768 devices in a mesh: sample: 32 (over z_lo, y), sect: 8 (over x, core), dom: 3 (over z_hi).
Axes of the slice: x: 4, y: 8, z: 12 (z_hi: 3, z_lo: 4; z = z_hi * 4 + z_lo), core: 2. Of those that a mesh axis runs over, the one named last changes fastest.
Arguments:
- features: bfloat16 [96, 512, 512], P(('sample', 'dom'), 'sect'), may hold values from -6 to 6
- weight: bfloat16 [4608, 512], P('sample', 'sect'), may hold values from -0.09375 to 0.09375
- style: float32 [96, 512], P(('sample', 'dom')), may hold values from 0.3 to 3
- bias: float32 [512], P('sect'), may hold values from -3 to 3
- adjoint: bfloat16 [96, 512, 512], P(('sample', 'dom'), 'sect'), may hold values from -6 to 6
Outputs:
- styled: bfloat16 [96, 512, 512], P(('sample', 'dom'), 'sect')
- grad_weight: float32 [4608, 512], P(('sample', 'dom'), 'sect')
- grad_features: bfloat16 [96, 512, 512], P(('sample', 'dom'), 'sect')
The draws below stay inside these ranges and needn't reach their ends.
All inputs are finite; a program needn't handle non-finite values.
Results may differ from the reference program's by a relative error of at most 0.0049.
Values may be sent and summed in bfloat16 or wider, within the bound.
No kernel may reach another device: no remote copies, remote signals or barrier semaphores. Data moves between devices by JAX's collectives and lax.ppermute only.
A program may use at most 32 MiB of HBM per device.

```python
import math
import jax
import jax.numpy as jnp
from jax import lax

CH = 512
WIDTH = 64
ROWS = 8
BATCH = 96


def level_of(own_key, shape, split, low, largest):
    loudness = 1.0
    for axis_at, shards_of in split:
        draws = jax.random.uniform(jax.random.fold_in(jax.random.fold_in(own_key, 6), axis_at), (shards_of,), jnp.float32, low / len(split), largest / len(split))
        loudness = loudness * jnp.repeat(jnp.exp(draws), shape[axis_at] // shards_of).reshape((-1,) + (1,) * (len(shape) - 1 - axis_at))
    return loudness


def scatter_about(own_key, shape, scale, limit, cuts=(), dtype=jnp.bfloat16):
    values = jax.random.normal(own_key, shape, jnp.float32) * scale
    if len(cuts) > 0:
        values = level_of(own_key, shape, cuts, -0.22, 0.18) * values
    return jnp.clip(values, min=-limit, max=limit).astype(dtype)


def setup_inputs(seed: int = 0) -> dict:
    streams_of = jax.random.split(jax.random.key(seed), 6)
    return {
        "features": scatter_about(streams_of[0], (BATCH, CH, ROWS * WIDTH), 1.0, 6.0, ((0, 96), (1, 8))),
        "weight": scatter_about(streams_of[1], (9 * CH, CH), (9 * CH) ** -0.5, 0.09375, ((0, 32), (1, 8))),
        "style": jnp.clip(jnp.exp(math.log(3.0) - 2.3025851 * jax.random.uniform(streams_of[2], (BATCH, CH), jnp.float32) ** level_of(streams_of[2], (BATCH, CH), ((0, 96),), -0.2, 0.2)), 0.3, 3.0),
        "bias": scatter_about(streams_of[3], (CH,), 0.5, 3.0, ((0, 8),), jnp.float32),
        "adjoint": scatter_about(streams_of[4], (BATCH, CH, ROWS * WIDTH), 1.0, 6.0, ((0, 96), (1, 8))),
    }


OFFSETS = [(-1, -1), (-1, 0), (-1, 1), (0, -1), (0, 0), (0, 1), (1, -1), (1, 0), (1, 1)]
EPSILON = 1e-08

def moved(array, row_step, col_step):
    count = array.shape[0]
    depth = array.shape[1]
    grid = array.reshape(count, depth, ROWS, WIDTH)
    padded = jnp.pad(grid, ((0, 0), (0, 0), (1, 1), (1, 1)))
    part = padded[:, :, 1 + row_step:1 + row_step + ROWS, 1 + col_step:1 + col_step + WIDTH]
    return part.reshape(count, depth, ROWS * WIDTH)

def reference(features, weight, style, bias, adjoint):
    channels = features.shape[1]
    modulated = (features.astype(jnp.float32) * style[:, :, None]).astype(jnp.bfloat16)
    kernel = weight.reshape(9, channels, channels)
    kernel_f = kernel.astype(jnp.float32)
    shifts = [moved(modulated, row_step, col_step).astype(jnp.float32) for row_step, col_step in OFFSETS]
    conv_out = jnp.zeros(features.shape, jnp.float32)
    for index in range(9):
        conv_out = conv_out + jnp.einsum('nip,io->nop', shifts[index], kernel_f[index])
    kernel_sq = lax.optimization_barrier(jnp.sum(kernel_f * kernel_f, axis=0))
    style_sq = style * style
    energy = jnp.dot(style_sq, kernel_sq, precision=lax.Precision.HIGHEST) + EPSILON
    demod = lax.rsqrt(energy)
    styled = (conv_out * demod[:, :, None] + bias[None, :, None]).astype(jnp.bfloat16)
    adjoint_f = adjoint.astype(jnp.float32)
    scaled_adjoint = (adjoint_f * demod[:, :, None]).astype(jnp.bfloat16)
    scaled_f = scaled_adjoint.astype(jnp.float32)
    demod_grad = lax.optimization_barrier(jnp.sum(adjoint_f * conv_out, axis=2))
    energy_grad = -0.5 * demod_grad * demod * demod * demod
    coupling = jnp.dot(style_sq.T, energy_grad, precision=lax.Precision.HIGHEST)
    grads = []
    back = jnp.zeros(features.shape, jnp.float32)
    for index in range(9):
        row_step, col_step = OFFSETS[index]
        grads.append(jnp.einsum('nip,nop->io', shifts[index], scaled_f) + 2.0 * kernel_f[index] * coupling)
        partial_back = jnp.einsum('nop,io->nip', scaled_f, kernel_f[index])
        back = back + moved(partial_back, -row_step, -col_step)
    grad_weight = jnp.concatenate(grads, axis=0)
    grad_features = (back * style[:, :, None]).astype(jnp.bfloat16)
    return (styled, grad_weight, grad_features)
```

```python
import jax
import jax.numpy as jnp
from jax import lax
from jax.sharding import PartitionSpec as P

WIDTH = 64
ROWS = 8


OFFSETS = [(-1, -1), (-1, 0), (-1, 1), (0, -1), (0, 0), (0, 1), (1, -1), (1, 0), (1, 1)]
EPSILON = 1e-08


def moved(array, row_step, col_step):
    count = array.shape[0]
    depth = array.shape[1]
    grid = array.reshape(count, depth, ROWS, WIDTH)
    padded = jnp.pad(grid, ((0, 0), (0, 0), (1, 1), (1, 1)))
    part = padded[:, :, 1 + row_step : 1 + row_step + ROWS, 1 + col_step : 1 + col_step + WIDTH]
    return part.reshape(count, depth, ROWS * WIDTH)


def gather_by_exchange(block, axis, count):
    copies = jnp.broadcast_to(block[None], (count,) + block.shape)
    return lax.all_to_all(copies, axis, 0, 0, tiled=True)


def sum_by_exchange(terms, axes):
    count = 1
    for axis in (axes if isinstance(axes, tuple) else (axes,)):
        count *= lax.axis_size(axis)
    blocks = terms.reshape((count, terms.shape[0] // count) + terms.shape[1:])
    return jnp.sum(lax.all_to_all(blocks, axes, 0, 0, tiled=True), axis=0)


def per_device(features, weight, style, bias, adjoint):
    local_ch = features.shape[1]
    sect_count = lax.axis_size("sect")
    sect_place = lax.axis_index("sect")
    channels = local_ch * sect_count
    samples = features.shape[0]
    pixels = features.shape[2]
    own_style = lax.dynamic_slice_in_dim(style, sect_place * local_ch, local_ch, 1)
    local_mod = (features.astype(jnp.float32) * own_style[:, :, None]).astype(jnp.bfloat16)
    gathered = gather_by_exchange(local_mod, "sect", sect_count)
    modulated = jnp.swapaxes(gathered, 0, 1).reshape(samples, channels, pixels)
    sample_count = lax.axis_size("sample")
    full_weight = gather_by_exchange(weight, "sample", sample_count).reshape(-1, local_ch)
    kernel = full_weight.reshape(9, channels, local_ch)
    kernel_f = kernel.astype(jnp.float32)
    shifts = [moved(modulated, row_step, col_step) for row_step, col_step in OFFSETS]
    conv_out = jnp.zeros(features.shape, jnp.float32)
    for index in range(9):
        conv_out = conv_out + jnp.einsum(
            "nip,io->nop", shifts[index], kernel[index], preferred_element_type=jnp.float32
        )
    kernel_sq = jnp.sum(kernel_f * kernel_f, axis=0)
    style_sq = style * style
    energy = jnp.dot(style_sq, kernel_sq, precision=lax.Precision.HIGHEST) + EPSILON
    demod = lax.rsqrt(energy)
    styled = (conv_out * demod[:, :, None] + bias[None, :, None]).astype(jnp.bfloat16)
    adjoint_f = adjoint.astype(jnp.float32)
    scaled_adjoint = (adjoint_f * demod[:, :, None]).astype(jnp.bfloat16)
    demod_grad = jnp.sum(adjoint_f * conv_out, axis=2)
    energy_grad = -0.5 * demod_grad * demod * demod * demod
    coupling = jnp.dot(style_sq.T, energy_grad, precision=lax.Precision.HIGHEST)
    grads = []
    for index in range(9):
        grads.append(
            jnp.einsum(
                "nip,nop->io", shifts[index], scaled_adjoint, preferred_element_type=jnp.float32
            )
            + 2.0 * kernel_f[index] * coupling
        )
    grad_terms = jnp.concatenate(grads, axis=0)
    grad_weight = sum_by_exchange(grad_terms, ("sample", "dom"))
    back = jnp.zeros((samples, channels, pixels), jnp.float32)
    for index in range(9):
        row_step, col_step = OFFSETS[index]
        partial_back = jnp.einsum(
            "nop,io->nip", scaled_adjoint, kernel[index], preferred_element_type=jnp.float32
        )
        back = back + moved(partial_back, -row_step, -col_step)
    by_owner = jnp.swapaxes(back.reshape(samples, sect_count, local_ch, pixels), 0, 1)
    summed = sum_by_exchange(by_owner.reshape(sect_count * samples, local_ch, pixels), "sect").reshape(samples, local_ch, pixels)
    grad_features = (summed * own_style[:, :, None]).astype(jnp.bfloat16)
    return (styled, grad_weight, grad_features)


def solution(mesh):
    in_specs = (
        P(("sample", "dom"), "sect", None),
        P("sample", "sect"),
        P(("sample", "dom"), None),
        P("sect"),
        P(("sample", "dom"), "sect", None),
    )
    out_specs = (
        P(("sample", "dom"), "sect", None),
        P(("sample", "dom"), "sect"),
        P(("sample", "dom"), "sect", None),
    )
    return jax.shard_map(
        per_device, mesh=mesh, in_specs=in_specs, out_specs=out_specs, check_vma=False
    )
```

```python
import jax
import jax.numpy as jnp
from jax import lax
from jax.sharding import PartitionSpec as P

WIDTH = 64
ROWS = 8


OFFSETS = [(-1, -1), (-1, 0), (-1, 1), (0, -1), (0, 0), (0, 1), (1, -1), (1, 0), (1, 1)]
EPSILON = 1e-08


def moved(array, row_step, col_step):
    pixels = array.shape[-1]
    step = row_step * WIDTH + col_step
    reach = WIDTH + 1
    padded = jnp.pad(array, [(0, 0)] * (array.ndim - 1) + [(reach, reach)])
    part = lax.slice_in_dim(padded, reach + step, reach + step + pixels, axis=array.ndim - 1)
    column = lax.broadcasted_iota(jnp.int32, array.shape, array.ndim - 1) % WIDTH
    inside = (column + col_step >= 0) & (column + col_step < WIDTH)
    return jnp.where(inside, part, jnp.zeros_like(part))


def gather_by_exchange(block, axis, count):
    copies = jnp.broadcast_to(block[None], (count,) + block.shape)
    return lax.all_to_all(copies, axis, 0, 0, tiled=True)


def sum_by_exchange(terms, axes):
    count = 1
    for axis in (axes if isinstance(axes, tuple) else (axes,)):
        count *= lax.axis_size(axis)
    blocks = terms.reshape((count, terms.shape[0] // count) + terms.shape[1:])
    return jnp.sum(lax.all_to_all(blocks, axes, 0, 0, tiled=True), axis=0)


def per_device(features, weight, style, bias, adjoint):
    local_ch = features.shape[1]
    sect_count = lax.axis_size("sect")
    sect_place = lax.axis_index("sect")
    channels = local_ch * sect_count
    samples = features.shape[0]
    pixels = features.shape[2]
    own_style = lax.dynamic_slice_in_dim(style, sect_place * local_ch, local_ch, 1)
    local_mod = (features.astype(jnp.float32) * own_style[:, :, None]).astype(jnp.bfloat16)
    gathered = gather_by_exchange(local_mod, "sect", sect_count)
    modulated = jnp.swapaxes(gathered, 0, 1).reshape(samples, channels, pixels)
    sample_count = lax.axis_size("sample")
    full_weight = gather_by_exchange(weight, "sample", sample_count).reshape(-1, local_ch)
    kernel = full_weight.reshape(9, channels, local_ch)
    kernel_f = kernel.astype(jnp.float32)
    products = jnp.einsum("kio,nip->nkop", kernel, modulated, preferred_element_type=jnp.float32)
    conv_out = moved(products[:, 0], *OFFSETS[0])
    for index in range(1, 9):
        conv_out = conv_out + moved(products[:, index], *OFFSETS[index])
    kernel_sq = jnp.sum(kernel_f * kernel_f, axis=0)
    style_sq = style * style
    energy = jnp.dot(style_sq, kernel_sq, precision=lax.Precision.HIGHEST) + EPSILON
    demod = lax.rsqrt(energy)
    styled = (conv_out * demod[:, :, None] + bias[None, :, None]).astype(jnp.bfloat16)
    adjoint_f = adjoint.astype(jnp.float32)
    scaled_adjoint = (adjoint_f * demod[:, :, None]).astype(jnp.bfloat16)
    demod_grad = jnp.sum(adjoint_f * conv_out, axis=2)
    energy_grad = -0.5 * demod_grad * demod * demod * demod
    coupling = jnp.dot(style_sq.T, energy_grad, precision=lax.Precision.HIGHEST)
    back_shifts = jnp.stack(
        [moved(scaled_adjoint, -row_step, -col_step) for row_step, col_step in OFFSETS], axis=1
    )
    grad_main = jnp.einsum("nip,nkop->kio", modulated, back_shifts, preferred_element_type=jnp.float32)
    grad_terms = (grad_main + 2.0 * kernel_f * coupling[None]).reshape(-1, local_ch)
    grad_weight = sum_by_exchange(grad_terms, ("sample", "dom"))
    back = jnp.einsum("kio,nkop->nip", kernel, back_shifts, preferred_element_type=jnp.float32)
    by_owner = jnp.swapaxes(back.reshape(samples, sect_count, local_ch, pixels), 0, 1)
    summed = sum_by_exchange(by_owner.reshape(sect_count * samples, local_ch, pixels), "sect").reshape(samples, local_ch, pixels)
    grad_features = (summed * own_style[:, :, None]).astype(jnp.bfloat16)
    return (styled, grad_weight, grad_features)


def solution(mesh):
    in_specs = (
        P(("sample", "dom"), "sect", None),
        P("sample", "sect"),
        P(("sample", "dom"), None),
        P("sect"),
        P(("sample", "dom"), "sect", None),
    )
    out_specs = (
        P(("sample", "dom"), "sect", None),
        P(("sample", "dom"), "sect"),
        P(("sample", "dom"), "sect", None),
    )
    return jax.shard_map(
        per_device, mesh=mesh, in_specs=in_specs, out_specs=out_specs, check_vma=False
    )
```

```python
import jax
import jax.numpy as jnp
from jax import lax
from jax.sharding import PartitionSpec as P

WIDTH = 64
ROWS = 8


OFFSETS = [(-1, -1), (-1, 0), (-1, 1), (0, -1), (0, 0), (0, 1), (1, -1), (1, 0), (1, 1)]
EPSILON = 1e-08


def moved(array, row_step, col_step):
    pixels = array.shape[-1]
    step = row_step * WIDTH + col_step
    reach = WIDTH + 1
    padded = jnp.pad(array, [(0, 0)] * (array.ndim - 1) + [(reach, reach)])
    part = lax.slice_in_dim(padded, reach + step, reach + step + pixels, axis=array.ndim - 1)
    column = lax.broadcasted_iota(jnp.int32, array.shape, array.ndim - 1) % WIDTH
    inside = (column + col_step >= 0) & (column + col_step < WIDTH)
    return jnp.where(inside, part, jnp.zeros_like(part))


def gather_by_exchange(block, axis, count):
    copies = jnp.broadcast_to(block[None], (count,) + block.shape)
    return lax.all_to_all(copies, axis, 0, 0, tiled=True)


def sum_by_exchange(terms, axes):
    count = 1
    for axis in (axes if isinstance(axes, tuple) else (axes,)):
        count *= lax.axis_size(axis)
    blocks = terms.reshape((count, terms.shape[0] // count) + terms.shape[1:])
    return jnp.sum(lax.all_to_all(blocks, axes, 0, 0, tiled=True), axis=0)


def gather_by_permutes(block, axis, count):
    place = lax.axis_index(axis)
    depth = block.shape[1]
    whole = jnp.zeros((block.shape[0], depth * count) + block.shape[2:], block.dtype)
    whole = lax.dynamic_update_slice_in_dim(whole, block, place * depth, 1)
    for distance in range(1, count):
        pairs = [(j, (j + distance) % count) for j in range(count)]
        arrived = lax.ppermute(block, axis, pairs)
        source = (place + count - distance) % count
        whole = lax.dynamic_update_slice_in_dim(whole, arrived, source * depth, 1)
    return whole


def sum_by_permutes(whole, axis, count):
    place = lax.axis_index(axis)
    depth = whole.shape[1] // count
    total = lax.dynamic_slice_in_dim(whole, place * depth, depth, 1)
    for distance in range(1, count):
        pairs = [(j, (j + distance) % count) for j in range(count)]
        target = (place + distance) % count
        part = lax.dynamic_slice_in_dim(whole, target * depth, depth, 1)
        total = total + lax.ppermute(part, axis, pairs)
    return total


def per_device(features, weight, style, bias, adjoint):
    local_ch = features.shape[1]
    sect_count = lax.axis_size("sect")
    sect_place = lax.axis_index("sect")
    channels = local_ch * sect_count
    samples = features.shape[0]
    pixels = features.shape[2]
    own_style = lax.dynamic_slice_in_dim(style, sect_place * local_ch, local_ch, 1)
    local_mod = (features.astype(jnp.float32) * own_style[:, :, None]).astype(jnp.bfloat16)
    modulated = gather_by_permutes(local_mod, "sect", sect_count)
    sample_count = lax.axis_size("sample")
    full_weight = gather_by_exchange(weight, "sample", sample_count).reshape(-1, local_ch)
    kernel = full_weight.reshape(9, channels, local_ch)
    kernel_f = kernel.astype(jnp.float32)
    products = jnp.einsum("kio,nip->nkop", kernel, modulated, preferred_element_type=jnp.float32)
    conv_out = moved(products[:, 0], *OFFSETS[0])
    for index in range(1, 9):
        conv_out = conv_out + moved(products[:, index], *OFFSETS[index])
    kernel_sq = jnp.sum(kernel_f * kernel_f, axis=0)
    style_sq = style * style
    energy = jnp.dot(style_sq, kernel_sq, precision=lax.Precision.HIGHEST) + EPSILON
    demod = lax.rsqrt(energy)
    styled = (conv_out * demod[:, :, None] + bias[None, :, None]).astype(jnp.bfloat16)
    adjoint_f = adjoint.astype(jnp.float32)
    scaled_adjoint = (adjoint_f * demod[:, :, None]).astype(jnp.bfloat16)
    demod_grad = jnp.sum(adjoint_f * conv_out, axis=2)
    energy_grad = -0.5 * demod_grad * demod * demod * demod
    coupling = jnp.dot(style_sq.T, energy_grad, precision=lax.Precision.HIGHEST)
    back_shifts = jnp.stack(
        [moved(scaled_adjoint, -row_step, -col_step) for row_step, col_step in OFFSETS], axis=1
    )
    grad_main = jnp.einsum("nip,nkop->kio", modulated, back_shifts, preferred_element_type=jnp.float32)
    grad_terms = (grad_main + 2.0 * kernel_f * coupling[None]).reshape(-1, local_ch)
    grad_weight = sum_by_exchange(grad_terms, ("sample", "dom"))
    back = jnp.einsum("kio,nkop->nip", kernel, back_shifts, preferred_element_type=jnp.float32)
    summed = sum_by_permutes(back, "sect", sect_count)
    grad_features = (summed * own_style[:, :, None]).astype(jnp.bfloat16)
    return (styled, grad_weight, grad_features)


def solution(mesh):
    in_specs = (
        P(("sample", "dom"), "sect", None),
        P("sample", "sect"),
        P(("sample", "dom"), None),
        P("sect"),
        P(("sample", "dom"), "sect", None),
    )
    out_specs = (
        P(("sample", "dom"), "sect", None),
        P(("sample", "dom"), "sect"),
        P(("sample", "dom"), "sect", None),
    )
    return jax.shard_map(
        per_device, mesh=mesh, in_specs=in_specs, out_specs=out_specs, check_vma=False
    )
```

```python
import jax
import jax.numpy as jnp
from jax import lax
from jax.sharding import Mesh, PartitionSpec as P

WIDTH = 64
ROWS = 8


OFFSETS = [(-1, -1), (-1, 0), (-1, 1), (0, -1), (0, 0), (0, 1), (1, -1), (1, 0), (1, 1)]
EPSILON = 1e-08


def moved(array, row_step, col_step):
    pixels = array.shape[-1]
    step = row_step * WIDTH + col_step
    reach = WIDTH + 1
    padded = jnp.pad(array, [(0, 0)] * (array.ndim - 1) + [(reach, reach)])
    part = lax.slice_in_dim(padded, reach + step, reach + step + pixels, axis=array.ndim - 1)
    column = lax.broadcasted_iota(jnp.int32, array.shape, array.ndim - 1) % WIDTH
    inside = (column + col_step >= 0) & (column + col_step < WIDTH)
    return jnp.where(inside, part, jnp.zeros_like(part))


def gather_by_exchange(block, axis, count):
    copies = jnp.broadcast_to(block[None], (count,) + block.shape)
    return lax.all_to_all(copies, axis, 0, 0, tiled=True)


def sum_by_exchange(terms, axes):
    count = 1
    for axis in (axes if isinstance(axes, tuple) else (axes,)):
        count *= lax.axis_size(axis)
    blocks = terms.reshape((count, terms.shape[0] // count) + terms.shape[1:])
    return jnp.sum(lax.all_to_all(blocks, axes, 0, 0, tiled=True), axis=0)


def gather_by_permutes(block, axis, count):
    place = lax.axis_index(axis)
    depth = block.shape[1]
    whole = jnp.zeros((block.shape[0], depth * count) + block.shape[2:], block.dtype)
    whole = lax.dynamic_update_slice_in_dim(whole, block, place * depth, 1)
    for distance in range(1, count):
        pairs = [(j, (j + distance) % count) for j in range(count)]
        arrived = lax.ppermute(block, axis, pairs)
        source = (place + count - distance) % count
        whole = lax.dynamic_update_slice_in_dim(whole, arrived, source * depth, 1)
    return whole


def sum_by_permutes(whole, axis, count):
    place = lax.axis_index(axis)
    depth = whole.shape[1] // count
    total = lax.dynamic_slice_in_dim(whole, place * depth, depth, 1)
    for distance in range(1, count):
        pairs = [(j, (j + distance) % count) for j in range(count)]
        target = (place + distance) % count
        part = lax.dynamic_slice_in_dim(whole, target * depth, depth, 1)
        total = total + lax.ppermute(part, axis, pairs)
    return total


SAMPLE = ("z_hi_half", "z_lo_half", "y_hi", "y_lo")
NEAR = ("z_lo_half", "y_lo")
FAR = ("z_hi_half", "y_hi", "dom")


def sum_in_two_stages(terms):
    sizes = {axis: lax.axis_size(axis) for axis in SAMPLE + ("dom",)}
    owners = terms.reshape([sizes[axis] for axis in SAMPLE + ("dom",)] + [-1, terms.shape[1]])
    order = SAMPLE + ("dom",)
    owners = jnp.transpose(owners, [order.index(axis) for axis in NEAR + FAR] + [5, 6])
    near = sizes[NEAR[0]] * sizes[NEAR[1]]
    owners = owners.reshape((near, -1) + owners.shape[-2:])
    partial = jnp.sum(lax.all_to_all(owners, NEAR, 0, 0, tiled=True), axis=0)
    return jnp.sum(lax.all_to_all(partial, FAR, 0, 0, tiled=True), axis=0)


def per_device(features, weight, style, bias, adjoint):
    local_ch = features.shape[1]
    sect_count = lax.axis_size("sect")
    sect_place = lax.axis_index("sect")
    channels = local_ch * sect_count
    samples = features.shape[0]
    pixels = features.shape[2]
    own_style = lax.dynamic_slice_in_dim(style, sect_place * local_ch, local_ch, 1)
    local_mod = (features.astype(jnp.float32) * own_style[:, :, None]).astype(jnp.bfloat16)
    modulated = gather_by_permutes(local_mod, "sect", sect_count)
    sample_count = 1
    for axis in SAMPLE:
        sample_count *= lax.axis_size(axis)
    full_weight = gather_by_exchange(weight, SAMPLE, sample_count).reshape(-1, local_ch)
    kernel = full_weight.reshape(9, channels, local_ch)
    kernel_f = kernel.astype(jnp.float32)
    products = jnp.einsum("kio,nip->nkop", kernel, modulated, preferred_element_type=jnp.float32)
    conv_out = moved(products[:, 0], *OFFSETS[0])
    for index in range(1, 9):
        conv_out = conv_out + moved(products[:, index], *OFFSETS[index])
    kernel_sq = jnp.sum(kernel_f * kernel_f, axis=0)
    style_sq = style * style
    energy = jnp.dot(style_sq, kernel_sq, precision=lax.Precision.HIGHEST) + EPSILON
    demod = lax.rsqrt(energy)
    styled = (conv_out * demod[:, :, None] + bias[None, :, None]).astype(jnp.bfloat16)
    adjoint_f = adjoint.astype(jnp.float32)
    scaled_adjoint = (adjoint_f * demod[:, :, None]).astype(jnp.bfloat16)
    demod_grad = jnp.sum(adjoint_f * conv_out, axis=2)
    energy_grad = -0.5 * demod_grad * demod * demod * demod
    coupling = jnp.dot(style_sq.T, energy_grad, precision=lax.Precision.HIGHEST)
    back_shifts = jnp.stack(
        [moved(scaled_adjoint, -row_step, -col_step) for row_step, col_step in OFFSETS], axis=1
    )
    grad_main = jnp.einsum("nip,nkop->kio", modulated, back_shifts, preferred_element_type=jnp.float32)
    grad_terms = (grad_main + 2.0 * kernel_f * coupling[None]).reshape(-1, local_ch)
    grad_weight = sum_in_two_stages(grad_terms)
    back = jnp.einsum("kio,nkop->nip", kernel, back_shifts, preferred_element_type=jnp.float32)
    summed = sum_by_permutes(back, "sect", sect_count)
    grad_features = (summed * own_style[:, :, None]).astype(jnp.bfloat16)
    return (styled, grad_weight, grad_features)


def solution(mesh):
    z_lo, y = 4, mesh.shape["sample"] // 4
    fine = Mesh(
        mesh.devices.reshape((2, z_lo // 2, y // 2, 2) + mesh.devices.shape[1:]),
        SAMPLE + ("sect", "dom"),
    )
    rows = SAMPLE + ("dom",)
    in_specs = (
        P(rows, "sect", None),
        P(SAMPLE, "sect"),
        P(rows, None),
        P("sect"),
        P(rows, "sect", None),
    )
    out_specs = (
        P(rows, "sect", None),
        P(rows, "sect"),
        P(rows, "sect", None),
    )
    return jax.shard_map(
        per_device, mesh=fine, in_specs=in_specs, out_specs=out_specs, check_vma=False
    )
```

```python
import jax
import jax.numpy as jnp
from jax import lax
from jax.sharding import PartitionSpec as P


WIDTH = 64


OFFSETS = [(-1, -1), (-1, 0), (-1, 1), (0, -1), (0, 0), (0, 1), (1, -1), (1, 0), (1, 1)]
EPSILON = 1e-08


def moved(array, row_step, col_step):
    pixels = array.shape[-1]
    step = row_step * WIDTH + col_step
    reach = WIDTH + 1
    padded = jnp.pad(array, [(0, 0)] * (array.ndim - 1) + [(reach, reach)])
    part = lax.slice_in_dim(padded, reach + step, reach + step + pixels, axis=array.ndim - 1)
    column = lax.broadcasted_iota(jnp.int32, array.shape, array.ndim - 1) % WIDTH
    inside = (column + col_step >= 0) & (column + col_step < WIDTH)
    return jnp.where(inside, part, jnp.zeros_like(part))


def gather_by_exchange(block, axis, count):
    copies = jnp.broadcast_to(block[None], (count,) + block.shape)
    return lax.all_to_all(copies, axis, 0, 0, tiled=True)


def sum_by_exchange(terms, axes):
    count = 1
    for axis in (axes if isinstance(axes, tuple) else (axes,)):
        count *= lax.axis_size(axis)
    blocks = terms.reshape((count, terms.shape[0] // count) + terms.shape[1:])
    return jnp.sum(lax.all_to_all(blocks, axes, 0, 0, tiled=True), axis=0)


def gather_by_permutes(block, axis, count):
    place = lax.axis_index(axis)
    depth = block.shape[1]
    whole = jnp.zeros((block.shape[0], depth * count) + block.shape[2:], block.dtype)
    whole = lax.dynamic_update_slice_in_dim(whole, block, place * depth, 1)
    for distance in range(1, count):
        pairs = [(j, (j + distance) % count) for j in range(count)]
        arrived = lax.ppermute(block, axis, pairs)
        source = (place + count - distance) % count
        whole = lax.dynamic_update_slice_in_dim(whole, arrived, source * depth, 1)
    return whole


def sum_by_permutes(whole, axis, count):
    place = lax.axis_index(axis)
    depth = whole.shape[1] // count
    total = lax.dynamic_slice_in_dim(whole, place * depth, depth, 1)
    for distance in range(1, count):
        pairs = [(j, (j + distance) % count) for j in range(count)]
        target = (place + distance) % count
        part = lax.dynamic_slice_in_dim(whole, target * depth, depth, 1)
        total = total + lax.ppermute(part, axis, pairs)
    return total


def layer(features, weight, style, bias, adjoint):
    local_ch = features.shape[1]
    sect_count = lax.axis_size("sect")
    sect_place = lax.axis_index("sect")
    channels = local_ch * sect_count
    own_style = lax.dynamic_slice_in_dim(style, sect_place * local_ch, local_ch, 1)
    local_mod = (features.astype(jnp.float32) * own_style[:, :, None]).astype(jnp.bfloat16)
    modulated = gather_by_permutes(local_mod, "sect", sect_count)
    sample_count = lax.axis_size("sample")
    full_weight = gather_by_exchange(weight, "sample", sample_count).reshape(-1, local_ch)
    kernel = full_weight.reshape(9, channels, local_ch)
    kernel_f = kernel.astype(jnp.float32)
    products = jnp.einsum("kio,nip->nkop", kernel, modulated, preferred_element_type=jnp.float32)
    conv_out = moved(products[:, 0], *OFFSETS[0])
    for index in range(1, 9):
        conv_out = conv_out + moved(products[:, index], *OFFSETS[index])
    kernel_sq = jnp.sum(kernel_f * kernel_f, axis=0)
    style_sq = style * style
    energy = jnp.dot(style_sq, kernel_sq, precision=lax.Precision.HIGHEST) + EPSILON
    demod = lax.rsqrt(energy)
    styled = (conv_out * demod[:, :, None] + bias[None, :, None]).astype(jnp.bfloat16)
    adjoint_f = adjoint.astype(jnp.float32)
    scaled_adjoint = (adjoint_f * demod[:, :, None]).astype(jnp.bfloat16)
    demod_grad = jnp.sum(adjoint_f * conv_out, axis=2)
    energy_grad = -0.5 * demod_grad * demod * demod * demod
    coupling = jnp.dot(style_sq.T, energy_grad, precision=lax.Precision.HIGHEST)
    back_shifts = jnp.stack(
        [moved(scaled_adjoint, -row_step, -col_step) for row_step, col_step in OFFSETS], axis=1
    )
    grad_main = jnp.einsum("nip,nkop->kio", modulated, back_shifts, preferred_element_type=jnp.float32)
    grad_terms = (grad_main + 2.0 * kernel_f * coupling[None]).reshape(-1, local_ch)
    grad_weight = sum_by_exchange(grad_terms, ("sample", "dom"))
    back = jnp.einsum("kio,nkop->nip", kernel, back_shifts, preferred_element_type=jnp.float32)
    summed = sum_by_permutes(back, "sect", sect_count)
    grad_features = (summed * own_style[:, :, None]).astype(jnp.bfloat16)
    return (styled, grad_weight, grad_features)


def solution(mesh):
    in_specs = (
        P(("sample", "dom"), "sect", None),
        P("sample", "sect"),
        P(("sample", "dom"), None),
        P("sect"),
        P(("sample", "dom"), "sect", None),
    )
    out_specs = (
        P(("sample", "dom"), "sect", None),
        P(("sample", "dom"), "sect"),
        P(("sample", "dom"), "sect", None),
    )
    return jax.shard_map(layer, mesh=mesh, in_specs=in_specs, out_specs=out_specs, check_vma=False)
```

```python
import jax
import jax.numpy as jnp
from jax import lax
from jax.sharding import Mesh, PartitionSpec as P


WIDTH = 64


OFFSETS = [(-1, -1), (-1, 0), (-1, 1), (0, -1), (0, 0), (0, 1), (1, -1), (1, 0), (1, 1)]
EPSILON = 1e-08
ROWS_AXES = ("z_lo", "y", "dom")


def moved(array, row_step, col_step):
    pixels = array.shape[-1]
    step = row_step * WIDTH + col_step
    reach = WIDTH + 1
    padded = jnp.pad(array, [(0, 0)] * (array.ndim - 1) + [(reach, reach)])
    part = lax.slice_in_dim(padded, reach + step, reach + step + pixels, axis=array.ndim - 1)
    column = lax.broadcasted_iota(jnp.int32, array.shape, array.ndim - 1) % WIDTH
    inside = (column + col_step >= 0) & (column + col_step < WIDTH)
    return jnp.where(inside, part, jnp.zeros_like(part))


def gather_by_exchange(block, axis, count):
    copies = jnp.broadcast_to(block[None], (count,) + block.shape)
    return lax.all_to_all(copies, axis, 0, 0, tiled=True)


def sum_by_exchange(terms, axes):
    count = 1
    for axis in (axes if isinstance(axes, tuple) else (axes,)):
        count *= lax.axis_size(axis)
    rows = terms.shape[0] // count
    flat = terms.reshape(count, rows * terms.shape[1])
    received = lax.all_to_all(flat, axes, 0, 0, tiled=True)
    return jnp.sum(received, axis=0).reshape(rows, terms.shape[1])


def gather_by_permutes(block, axis, count):
    place = lax.axis_index(axis)
    depth = block.shape[1]
    whole = jnp.zeros((block.shape[0], depth * count) + block.shape[2:], block.dtype)
    whole = lax.dynamic_update_slice_in_dim(whole, block, place * depth, 1)
    for distance in range(1, count):
        pairs = [(j, (j + distance) % count) for j in range(count)]
        arrived = lax.ppermute(block, axis, pairs)
        source = (place + count - distance) % count
        whole = lax.dynamic_update_slice_in_dim(whole, arrived, source * depth, 1)
    return whole


def sum_by_permutes(whole, axis, count):
    place = lax.axis_index(axis)
    depth = whole.shape[1] // count
    total = lax.dynamic_slice_in_dim(whole, place * depth, depth, 1)
    for distance in range(1, count):
        pairs = [(j, (j + distance) % count) for j in range(count)]
        target = (place + distance) % count
        part = lax.dynamic_slice_in_dim(whole, target * depth, depth, 1)
        total = total + lax.ppermute(part, axis, pairs)
    return total


def layer(features, weight, style, bias, adjoint):
    local_ch = features.shape[1]
    sect_count = lax.axis_size("sect")
    sect_place = lax.axis_index("sect")
    channels = local_ch * sect_count
    own_style = lax.dynamic_slice_in_dim(style, sect_place * local_ch, local_ch, 1)
    local_mod = (features.astype(jnp.float32) * own_style[:, :, None]).astype(jnp.bfloat16)
    modulated = gather_by_permutes(local_mod, "sect", sect_count)
    along_y = gather_by_exchange(weight, "y", lax.axis_size("y"))
    full_weight = gather_by_exchange(along_y, "z_lo", lax.axis_size("z_lo")).reshape(-1, local_ch)
    kernel = full_weight.reshape(9, channels, local_ch)
    kernel_f = kernel.astype(jnp.float32)
    products = jnp.einsum("kio,nip->nkop", kernel, modulated, preferred_element_type=jnp.float32)
    conv_out = moved(products[:, 0], *OFFSETS[0])
    for index in range(1, 9):
        conv_out = conv_out + moved(products[:, index], *OFFSETS[index])
    kernel_sq = jnp.sum(kernel_f * kernel_f, axis=0)
    style_sq = style * style
    energy = jnp.dot(style_sq, kernel_sq, precision=lax.Precision.HIGHEST) + EPSILON
    demod = lax.rsqrt(energy)
    styled = (conv_out * demod[:, :, None] + bias[None, :, None]).astype(jnp.bfloat16)
    adjoint_f = adjoint.astype(jnp.float32)
    scaled_adjoint = (adjoint_f * demod[:, :, None]).astype(jnp.bfloat16)
    demod_grad = jnp.sum(adjoint_f * conv_out, axis=2)
    energy_grad = -0.5 * demod_grad * demod * demod * demod
    coupling = jnp.dot(style_sq.T, energy_grad, precision=lax.Precision.HIGHEST)
    back_shifts = jnp.stack(
        [moved(scaled_adjoint, -row_step, -col_step) for row_step, col_step in OFFSETS], axis=1
    )
    grad_main = jnp.einsum("nip,nkop->kio", modulated, back_shifts, preferred_element_type=jnp.float32)
    grad_terms = (grad_main + 2.0 * kernel_f * coupling[None]).reshape(-1, local_ch)
    grad_weight = sum_by_exchange(grad_terms, ROWS_AXES)
    back = jnp.einsum("kio,nkop->nip", kernel, back_shifts, preferred_element_type=jnp.float32)
    summed = sum_by_permutes(back, "sect", sect_count)
    grad_features = (summed * own_style[:, :, None]).astype(jnp.bfloat16)
    return (styled, grad_weight, grad_features)


def solution(mesh):
    z_lo = 4
    fine = Mesh(
        mesh.devices.reshape((z_lo, mesh.shape["sample"] // z_lo) + mesh.devices.shape[1:]),
        ("z_lo", "y", "sect", "dom"),
    )
    in_specs = (
        P(ROWS_AXES, "sect", None),
        P(("z_lo", "y"), "sect"),
        P(ROWS_AXES, None),
        P("sect"),
        P(ROWS_AXES, "sect", None),
    )
    out_specs = (
        P(ROWS_AXES, "sect", None),
        P(ROWS_AXES, "sect"),
        P(ROWS_AXES, "sect", None),
    )
    return jax.shard_map(layer, mesh=fine, in_specs=in_specs, out_specs=out_specs, check_vma=False)
```

```python
import jax
import jax.numpy as jnp
from jax import lax
from jax.sharding import Mesh, PartitionSpec as P


WIDTH = 64


OFFSETS = [(-1, -1), (-1, 0), (-1, 1), (0, -1), (0, 0), (0, 1), (1, -1), (1, 0), (1, 1)]
EPSILON = 1e-08
SECT = ("sect_x", "sect_core")


def moved(array, row_step, col_step):
    pixels = array.shape[-1]
    step = row_step * WIDTH + col_step
    reach = WIDTH + 1
    padded = jnp.pad(array, [(0, 0)] * (array.ndim - 1) + [(reach, reach)])
    part = lax.slice_in_dim(padded, reach + step, reach + step + pixels, axis=array.ndim - 1)
    column = lax.broadcasted_iota(jnp.int32, array.shape, array.ndim - 1) % WIDTH
    inside = (column + col_step >= 0) & (column + col_step < WIDTH)
    return jnp.where(inside, part, jnp.zeros_like(part))


def gather_by_exchange(block, axis, count):
    copies = jnp.broadcast_to(block[None], (count,) + block.shape)
    return lax.all_to_all(copies, axis, 0, 0, tiled=True)


def sum_by_exchange(terms, axes):
    count = 1
    for axis in (axes if isinstance(axes, tuple) else (axes,)):
        count *= lax.axis_size(axis)
    rows = terms.shape[0] // count
    flat = terms.reshape(count, rows * terms.shape[1])
    received = lax.all_to_all(flat, axes, 0, 0, tiled=True)
    return jnp.sum(received, axis=0).reshape(rows, terms.shape[1])


def gather_by_permutes(block, axis, count, place):
    depth = block.shape[1]
    whole = jnp.zeros((block.shape[0], depth * count) + block.shape[2:], block.dtype)
    whole = lax.dynamic_update_slice_in_dim(whole, block, place * depth, 1)
    for distance in range(1, count):
        pairs = [(j, (j + distance) % count) for j in range(count)]
        arrived = lax.ppermute(block, axis, pairs)
        source = (place + count - distance) % count
        whole = lax.dynamic_update_slice_in_dim(whole, arrived, source * depth, 1)
    return whole


def sum_core_then_x(whole):
    samples, channels, pixels = whole.shape
    chips, cores = lax.axis_size("sect_x"), lax.axis_size("sect_core")
    depth = channels // (chips * cores)
    core = lax.axis_index("sect_core")
    chip = lax.axis_index("sect_x")
    grid = whole.reshape(samples, chips, cores, depth, pixels)
    mine = lax.dynamic_index_in_dim(grid, core, 2, keepdims=False)
    other = lax.dynamic_index_in_dim(grid, 1 - core, 2, keepdims=False)
    partial = mine + lax.ppermute(other, "sect_core", [(0, 1), (1, 0)])
    total = lax.dynamic_index_in_dim(partial, chip, 1, keepdims=False)
    for distance in range(1, chips):
        pairs = [(j, (j + distance) % chips) for j in range(chips)]
        part = lax.dynamic_index_in_dim(partial, (chip + distance) % chips, 1, keepdims=False)
        total = total + lax.ppermute(part, "sect_x", pairs)
    return total


def layer(features, weight, style, bias, adjoint):
    local_ch = features.shape[1]
    sect_count = lax.axis_size(SECT)
    sect_place = lax.axis_index("sect_x") * lax.axis_size("sect_core") + lax.axis_index("sect_core")
    channels = local_ch * sect_count
    own_style = lax.dynamic_slice_in_dim(style, sect_place * local_ch, local_ch, 1)
    local_mod = (features.astype(jnp.float32) * own_style[:, :, None]).astype(jnp.bfloat16)
    modulated = gather_by_permutes(local_mod, SECT, sect_count, sect_place)
    sample_count = lax.axis_size("sample")
    full_weight = gather_by_exchange(weight, "sample", sample_count).reshape(-1, local_ch)
    kernel = full_weight.reshape(9, channels, local_ch)
    kernel_f = kernel.astype(jnp.float32)
    products = jnp.einsum("kio,nip->nkop", kernel, modulated, preferred_element_type=jnp.float32)
    conv_out = moved(products[:, 0], *OFFSETS[0])
    for index in range(1, 9):
        conv_out = conv_out + moved(products[:, index], *OFFSETS[index])
    kernel_sq = jnp.sum(kernel_f * kernel_f, axis=0)
    style_sq = style * style
    energy = jnp.dot(style_sq, kernel_sq, precision=lax.Precision.HIGHEST) + EPSILON
    demod = lax.rsqrt(energy)
    styled = (conv_out * demod[:, :, None] + bias[None, :, None]).astype(jnp.bfloat16)
    adjoint_f = adjoint.astype(jnp.float32)
    scaled_adjoint = (adjoint_f * demod[:, :, None]).astype(jnp.bfloat16)
    demod_grad = jnp.sum(adjoint_f * conv_out, axis=2)
    energy_grad = -0.5 * demod_grad * demod * demod * demod
    coupling = jnp.dot(style_sq.T, energy_grad, precision=lax.Precision.HIGHEST)
    back_shifts = jnp.stack(
        [moved(scaled_adjoint, -row_step, -col_step) for row_step, col_step in OFFSETS], axis=1
    )
    grad_main = jnp.einsum("nip,nkop->kio", modulated, back_shifts, preferred_element_type=jnp.float32)
    grad_terms = (grad_main + 2.0 * kernel_f * coupling[None]).reshape(-1, local_ch)
    grad_weight = sum_by_exchange(grad_terms, ("sample", "dom"))
    back = jnp.einsum("kio,nkop->nip", kernel, back_shifts, preferred_element_type=jnp.float32)
    summed = sum_core_then_x(back)
    grad_features = (summed * own_style[:, :, None]).astype(jnp.bfloat16)
    return (styled, grad_weight, grad_features)


def solution(mesh):
    cores = 2
    fine = Mesh(
        mesh.devices.reshape(
            (mesh.shape["sample"], mesh.shape["sect"] // cores, cores, mesh.shape["dom"])
        ),
        ("sample",) + SECT + ("dom",),
    )
    in_specs = (
        P(("sample", "dom"), SECT, None),
        P("sample", SECT),
        P(("sample", "dom"), None),
        P(SECT),
        P(("sample", "dom"), SECT, None),
    )
    out_specs = (
        P(("sample", "dom"), SECT, None),
        P(("sample", "dom"), SECT),
        P(("sample", "dom"), SECT, None),
    )
    return jax.shard_map(layer, mesh=fine, in_specs=in_specs, out_specs=out_specs, check_vma=False)
```

```python
import jax
import jax.numpy as jnp
from jax import lax
from jax.sharding import Mesh, PartitionSpec as P


WIDTH = 64


OFFSETS = [(-1, -1), (-1, 0), (-1, 1), (0, -1), (0, 0), (0, 1), (1, -1), (1, 0), (1, 1)]
EPSILON = 1e-08
ROWS_AXES = ("z_lo", "y", "dom")


def moved(array, row_step, col_step):
    pixels = array.shape[-1]
    step = row_step * WIDTH + col_step
    reach = WIDTH + 1
    padded = jnp.pad(array, [(0, 0)] * (array.ndim - 1) + [(reach, reach)])
    part = lax.slice_in_dim(padded, reach + step, reach + step + pixels, axis=array.ndim - 1)
    column = lax.broadcasted_iota(jnp.int32, array.shape, array.ndim - 1) % WIDTH
    inside = (column + col_step >= 0) & (column + col_step < WIDTH)
    return jnp.where(inside, part, jnp.zeros_like(part))


def gather_by_exchange(block, axis, count):
    copies = jnp.broadcast_to(block[None], (count,) + block.shape)
    return lax.all_to_all(copies, axis, 0, 0, tiled=True)


def gather_by_permutes(block, axis, count):
    place = lax.axis_index(axis)
    depth = block.shape[1]
    whole = jnp.zeros((block.shape[0], depth * count) + block.shape[2:], block.dtype)
    whole = lax.dynamic_update_slice_in_dim(whole, block, place * depth, 1)
    for distance in range(1, count):
        pairs = [(j, (j + distance) % count) for j in range(count)]
        arrived = lax.ppermute(block, axis, pairs)
        source = (place + count - distance) % count
        whole = lax.dynamic_update_slice_in_dim(whole, arrived, source * depth, 1)
    return whole


def sum_by_permutes(whole, axis, count):
    place = lax.axis_index(axis)
    depth = whole.shape[1] // count
    total = lax.dynamic_slice_in_dim(whole, place * depth, depth, 1)
    for distance in range(1, count):
        pairs = [(j, (j + distance) % count) for j in range(count)]
        target = (place + distance) % count
        part = lax.dynamic_slice_in_dim(whole, target * depth, depth, 1)
        total = total + lax.ppermute(part, axis, pairs)
    return total


def sum_along_y_then_z(terms):
    z_lo, y, dom = (lax.axis_size(axis) for axis in ROWS_AXES)
    rows, cols = terms.shape[0] // (z_lo * y * dom), terms.shape[1]
    owners = jnp.swapaxes(terms.reshape(z_lo, y, dom, rows * cols), 0, 1).reshape(y, -1)
    along_y = jnp.sum(lax.all_to_all(owners, "y", 0, 0, tiled=True), axis=0)
    along_z = lax.all_to_all(along_y.reshape(z_lo * dom, rows * cols), ("z_lo", "dom"), 0, 0, tiled=True)
    return jnp.sum(along_z, axis=0).reshape(rows, cols)


def layer(features, weight, style, bias, adjoint):
    local_ch = features.shape[1]
    sect_count = lax.axis_size("sect")
    sect_place = lax.axis_index("sect")
    channels = local_ch * sect_count
    own_style = lax.dynamic_slice_in_dim(style, sect_place * local_ch, local_ch, 1)
    local_mod = (features.astype(jnp.float32) * own_style[:, :, None]).astype(jnp.bfloat16)
    modulated = gather_by_permutes(local_mod, "sect", sect_count)
    sample_count = lax.axis_size("z_lo") * lax.axis_size("y")
    full_weight = gather_by_exchange(weight, ("z_lo", "y"), sample_count).reshape(-1, local_ch)
    kernel = full_weight.reshape(9, channels, local_ch)
    kernel_f = kernel.astype(jnp.float32)
    products = jnp.einsum("kio,nip->nkop", kernel, modulated, preferred_element_type=jnp.float32)
    conv_out = moved(products[:, 0], *OFFSETS[0])
    for index in range(1, 9):
        conv_out = conv_out + moved(products[:, index], *OFFSETS[index])
    kernel_sq = jnp.sum(kernel_f * kernel_f, axis=0)
    style_sq = style * style
    energy = jnp.dot(style_sq, kernel_sq, precision=lax.Precision.HIGHEST) + EPSILON
    demod = lax.rsqrt(energy)
    styled = (conv_out * demod[:, :, None] + bias[None, :, None]).astype(jnp.bfloat16)
    adjoint_f = adjoint.astype(jnp.float32)
    scaled_adjoint = (adjoint_f * demod[:, :, None]).astype(jnp.bfloat16)
    demod_grad = jnp.sum(adjoint_f * conv_out, axis=2)
    energy_grad = -0.5 * demod_grad * demod * demod * demod
    coupling = jnp.dot(style_sq.T, energy_grad, precision=lax.Precision.HIGHEST)
    back_shifts = jnp.stack(
        [moved(scaled_adjoint, -row_step, -col_step) for row_step, col_step in OFFSETS], axis=1
    )
    grad_main = jnp.einsum("nip,nkop->kio", modulated, back_shifts, preferred_element_type=jnp.float32)
    grad_terms = (grad_main + 2.0 * kernel_f * coupling[None]).reshape(-1, local_ch)
    grad_weight = sum_along_y_then_z(grad_terms)
    back = jnp.einsum("kio,nkop->nip", kernel, back_shifts, preferred_element_type=jnp.float32)
    summed = sum_by_permutes(back, "sect", sect_count)
    grad_features = (summed * own_style[:, :, None]).astype(jnp.bfloat16)
    return (styled, grad_weight, grad_features)


def solution(mesh):
    z_lo = 4
    fine = Mesh(
        mesh.devices.reshape((z_lo, mesh.shape["sample"] // z_lo) + mesh.devices.shape[1:]),
        ("z_lo", "y", "sect", "dom"),
    )
    in_specs = (
        P(ROWS_AXES, "sect", None),
        P(("z_lo", "y"), "sect"),
        P(ROWS_AXES, None),
        P("sect"),
        P(ROWS_AXES, "sect", None),
    )
    out_specs = (
        P(ROWS_AXES, "sect", None),
        P(ROWS_AXES, "sect"),
        P(ROWS_AXES, "sect", None),
    )
    return jax.shard_map(layer, mesh=fine, in_specs=in_specs, out_specs=out_specs, check_vma=False)
```

```python
import jax
import jax.numpy as jnp
from jax import lax
from jax.sharding import PartitionSpec as P


WIDTH = 64


OFFSETS = [(-1, -1), (-1, 0), (-1, 1), (0, -1), (0, 0), (0, 1), (1, -1), (1, 0), (1, 1)]
EPSILON = 1e-08


def moved(array, row_step, col_step):
    pixels = array.shape[-1]
    step = row_step * WIDTH + col_step
    reach = WIDTH + 1
    padded = jnp.pad(array, [(0, 0)] * (array.ndim - 1) + [(reach, reach)])
    part = lax.slice_in_dim(padded, reach + step, reach + step + pixels, axis=array.ndim - 1)
    column = lax.broadcasted_iota(jnp.int32, array.shape, array.ndim - 1) % WIDTH
    inside = (column + col_step >= 0) & (column + col_step < WIDTH)
    return jnp.where(inside, part, jnp.zeros_like(part))


def gather_by_exchange(block, axis, count):
    copies = jnp.broadcast_to(block[None], (count,) + block.shape)
    return lax.all_to_all(copies, axis, 0, 0, tiled=True)


def sum_by_exchange(terms, axes):
    count = 1
    for axis in (axes if isinstance(axes, tuple) else (axes,)):
        count *= lax.axis_size(axis)
    rows = terms.shape[0] // count
    flat = terms.reshape(count, rows * terms.shape[1])
    received = lax.all_to_all(flat, axes, 0, 0, tiled=True)
    return jnp.sum(received, axis=0).reshape(rows, terms.shape[1])


def gather_by_permutes(block, axis, count):
    place = lax.axis_index(axis)
    depth = block.shape[1]
    whole = jnp.zeros((block.shape[0], depth * count) + block.shape[2:], block.dtype)
    whole = lax.dynamic_update_slice_in_dim(whole, block, place * depth, 1)
    for distance in range(1, count):
        pairs = [(j, (j + distance) % count) for j in range(count)]
        arrived = lax.ppermute(block, axis, pairs)
        source = (place + count - distance) % count
        whole = lax.dynamic_update_slice_in_dim(whole, arrived, source * depth, 1)
    return whole


def sum_by_permutes(whole, axis, count):
    place = lax.axis_index(axis)
    depth = whole.shape[1] // count
    total = lax.dynamic_slice_in_dim(whole, place * depth, depth, 1)
    for distance in range(1, count):
        pairs = [(j, (j + distance) % count) for j in range(count)]
        target = (place + distance) % count
        part = lax.dynamic_slice_in_dim(whole, target * depth, depth, 1)
        total = total + lax.ppermute(part, axis, pairs)
    return total


def layer(features, weight, style, bias, adjoint):
    local_ch = features.shape[1]
    sect_count = lax.axis_size("sect")
    sect_place = lax.axis_index("sect")
    channels = local_ch * sect_count
    own_style = lax.dynamic_slice_in_dim(style, sect_place * local_ch, local_ch, 1)
    local_mod = (features.astype(jnp.float32) * own_style[:, :, None]).astype(jnp.bfloat16)
    modulated = gather_by_permutes(local_mod, "sect", sect_count)
    sample_count = lax.axis_size("sample")
    full_weight = gather_by_exchange(weight.reshape(-1), "sample", sample_count).reshape(-1, local_ch)
    kernel = full_weight.reshape(9, channels, local_ch)
    kernel_f = kernel.astype(jnp.float32)
    products = jnp.einsum("kio,nip->nkop", kernel, modulated, preferred_element_type=jnp.float32)
    conv_out = moved(products[:, 0], *OFFSETS[0])
    for index in range(1, 9):
        conv_out = conv_out + moved(products[:, index], *OFFSETS[index])
    kernel_sq = jnp.sum(kernel_f * kernel_f, axis=0)
    style_sq = style * style
    energy = jnp.dot(style_sq, kernel_sq, precision=lax.Precision.HIGHEST) + EPSILON
    demod = lax.rsqrt(energy)
    styled = (conv_out * demod[:, :, None] + bias[None, :, None]).astype(jnp.bfloat16)
    adjoint_f = adjoint.astype(jnp.float32)
    scaled_adjoint = (adjoint_f * demod[:, :, None]).astype(jnp.bfloat16)
    demod_grad = jnp.sum(adjoint_f * conv_out, axis=2)
    energy_grad = -0.5 * demod_grad * demod * demod * demod
    coupling = jnp.dot(style_sq.T, energy_grad, precision=lax.Precision.HIGHEST)
    back_shifts = jnp.stack(
        [moved(scaled_adjoint, -row_step, -col_step) for row_step, col_step in OFFSETS], axis=1
    )
    grad_main = jnp.einsum("nip,nkop->kio", modulated, back_shifts, preferred_element_type=jnp.float32)
    grad_terms = (grad_main + 2.0 * kernel_f * coupling[None]).reshape(-1, local_ch)
    grad_weight = sum_by_exchange(grad_terms, ("sample", "dom"))
    back = jnp.einsum("kio,nkop->nip", kernel, back_shifts, preferred_element_type=jnp.float32)
    summed = sum_by_permutes(back, "sect", sect_count)
    grad_features = (summed * own_style[:, :, None]).astype(jnp.bfloat16)
    return (styled, grad_weight, grad_features)


def solution(mesh):
    in_specs = (
        P(("sample", "dom"), "sect", None),
        P("sample", "sect"),
        P(("sample", "dom"), None),
        P("sect"),
        P(("sample", "dom"), "sect", None),
    )
    out_specs = (
        P(("sample", "dom"), "sect", None),
        P(("sample", "dom"), "sect"),
        P(("sample", "dom"), "sect", None),
    )
    return jax.shard_map(layer, mesh=mesh, in_specs=in_specs, out_specs=out_specs, check_vma=False)
```
